1024 devices in a mesh: ctx: 64 (over z, core), head: 16 (over y, x).
Axes of the slice: x: 4, y: 4, z: 32, core: 2. Of those that a mesh axis runs over, the one named last changes fastest.
Arguments:
- queries: bfloat16 [32768, 8192], P('ctx', 'head'), may hold values from -136 to 136
- keys: bfloat16 [32768, 8192], P('ctx', 'head'), may hold values from -6 to 6
- values: bfloat16 [32768, 8192], P('ctx', 'head'), may hold values from -6 to 6
- segment_ids: int32 [32768], P('ctx'), may hold values from 0 to 3, never falling along the last dimension, each value on 1 to 16384 neighbouring positions
Outputs:
- attended: bfloat16 [32768, 8192], P('ctx', 'head')
The draws below stay inside these ranges and needn't reach their ends.
Inputs may be any that keep to these rules, and one draw needn't show every extreme that they name: `segment_ids`: document numbers never fall along the tokens; every document of 0 to 3 appears, with 1 to 16384 tokens, one with exactly 16384.
All inputs are finite; a program needn't handle non-finite values.
Results may differ from the reference program's by a relative error of at most 0.0049.
Values may be sent and summed in bfloat16 or wider, within the bound.
No kernel may reach another device: no remote copies, remote signals or barrier semaphores. Data moves between devices by JAX's collectives and lax.ppermute only.
A program may use at most 64 MiB of HBM per device.

```python
import math
import jax
import jax.numpy as jnp
import numpy as np
from jax import lax

HEADS = 64
DH = 128
BLK = 512
DOCS = 4
TOKENS = 32768
SEG_MOST = 16384


def draw_queries(key, part):
    key_base = jax.random.fold_in(key, 11)
    key_head = jax.random.fold_in(key, 12)
    head_scale = jnp.exp(jax.random.uniform(key_head, (HEADS,), jnp.float32) * math.log(10.0))
    base = jnp.clip(jax.random.normal(key_base, (TOKENS, HEADS, DH), jnp.float32), -6.0, 6.0)
    full = base * head_scale[None, :, None]
    return full.reshape(TOKENS, HEADS * DH).astype(jnp.bfloat16)


def block_levels(key, dims, cuts, smallest, largest):
    gain, own = 1.0, jax.random.fold_in(key, 6)
    for dim, shards_of in cuts:
        steps = jnp.exp(jax.random.uniform(jax.random.fold_in(own, dim), (shards_of,), jnp.float32, smallest / len(cuts), largest / len(cuts)))
        gain = gain * jnp.repeat(steps, dims[dim] // shards_of).reshape([-1 if axis == dim else 1 for axis in range(len(dims))])
    return gain


def profile(number_of, total, reach, skew):
    portions = [(1 << 20) // math.isqrt(standing ** skew) + 1 for standing in range(2, number_of + 1)]
    rest, holding = total - reach - (number_of - 1), [1] * (number_of - 1)
    while rest > 0:
        free = [i for i in range(number_of - 1) if holding[i] < reach]
        pool, budget = sum([portions[i] for i in free]), rest
        for i in free:
            addition = min(reach - holding[i], max(1, budget * portions[i] // pool), rest)
            holding[i] = holding[i] + addition
            rest = rest - addition
    return np.array([reach] + holding)


def ragged(stream_key, amount, total, reach, slope):
    if amount == 2:
        one = jax.random.randint(stream_key, (), max(1, total - reach), min(reach, total - 1) + 1)
        return jnp.stack([one, total - one])
    lengths = jnp.asarray(profile(amount, total, reach, slope), jnp.int32)
    couples = (amount - 1) // 2
    donor, sink = lengths[1:1 + 2 * couples:2], lengths[2:2 + 2 * couples:2]
    slack = jnp.minimum(donor - 1, reach - sink)
    moved = jax.random.randint(jax.random.fold_in(stream_key, 1), (couples,), 0, 1 << 20) % (slack + 1)
    lengths = lengths.at[1:1 + 2 * couples:2].set(donor - moved).at[2:2 + 2 * couples:2].set(sink + moved)
    return lengths[jax.random.permutation(jax.random.fold_in(stream_key, 2), amount)]


def normal_values(rng, extent, width, limit, shards=(), held_as=jnp.bfloat16):
    result = jax.random.normal(rng, extent, jnp.float32) * width
    if len(shards) > 0:
        result = block_levels(rng, extent, shards, -0.22, 0.18) * result
    return jnp.clip(result, min=-limit, max=limit).astype(held_as)


def setup_inputs(seed: int = 0) -> dict:
    key_of = jax.random.split(jax.random.key(seed), 5)
    return {
        "queries": draw_queries(jax.random.fold_in(key_of[4], 71), 0),
        "keys": normal_values(key_of[1], (TOKENS, HEADS * DH), 1.0, 6.0, ((0, 64), (1, 16))),
        "values": normal_values(key_of[2], (TOKENS, HEADS * DH), 1.0, 6.0, ((0, 64), (1, 16))),
        "segment_ids": jnp.searchsorted(jnp.cumsum(ragged(key_of[3], DOCS, TOKENS, SEG_MOST, 0)), jnp.arange(TOKENS), side="right").astype(jnp.int32),
    }


def reference(queries, keys, values, segment_ids):
    blocks = TOKENS // BLK
    q_all = queries.reshape(blocks, BLK, HEADS, DH)
    k_all = keys.reshape(blocks, BLK, HEADS, DH)
    v_all = values.reshape(blocks, BLK, HEADS, DH)
    s_all = segment_ids.reshape(blocks, BLK)
    rows = jnp.arange(BLK)
    causal = rows[:, None] >= rows[None, :]

    def step(carry, item):
        state, last = carry
        qb, kb, vb, sb = item
        scores = jnp.einsum('thd,shd->hts', qb.astype(jnp.float32), kb.astype(jnp.float32))
        mask = causal & (sb[:, None] == sb[None, :])
        probs = jnp.where(mask[None], scores, 0.0).astype(jnp.bfloat16)
        intra = jnp.einsum('hts,shd->thd', probs.astype(jnp.float32), vb.astype(jnp.float32))
        state_b = state.astype(jnp.bfloat16).astype(jnp.float32)
        inter = jnp.einsum('thd,hde->the', qb.astype(jnp.float32), state_b)
        inter = jnp.where((sb == last)[:, None, None], inter, 0.0)
        block_last = sb[-1]
        keep = (sb == block_last)[:, None, None]
        kv = jnp.einsum('thd,the->hde', jnp.where(keep, kb, jnp.zeros_like(kb)).astype(jnp.float32), vb.astype(jnp.float32))
        new_state = jnp.where(last == block_last, state, jnp.zeros_like(state)) + kv
        return ((new_state, block_last), intra + inter)
    init = (jnp.zeros((HEADS, DH, DH), jnp.float32), jnp.int32(-1))
    _, outs = lax.scan(step, init, (q_all, k_all, v_all, s_all))
    outs = outs.reshape(TOKENS, HEADS * DH)
    mean_sq = lax.optimization_barrier(jnp.sum(outs * outs, axis=1)) / (HEADS * DH)
    return (outs * lax.rsqrt(mean_sq + 1e-05)[:, None]).astype(jnp.bfloat16)
```

```python
import jax
import jax.numpy as jnp
from jax import lax
from jax.sharding import PartitionSpec as P

HEADS = 64
DH = 128
BLK = 512


def combine_states(earlier, later):
    state_e, last_e = earlier
    state_l, last_l = later
    joined = state_l + jnp.where(last_e == last_l, state_e, jnp.zeros_like(state_e))
    state = jnp.where(last_l < 0, state_e, joined)
    last = jnp.where(last_l < 0, last_e, last_l)
    return (state, last)


def carried_in(own, axis):
    count, mine = (lax.axis_size(axis), lax.axis_index(axis))
    state, last = own
    excl = (jnp.zeros_like(state), jnp.full_like(last, -1))
    incl = (state, last)
    shift = 1
    while shift < count:
        pairs = [(j, j + shift) for j in range(count - shift)]
        got_state, got_last = lax.ppermute(incl, axis, pairs)
        got_last = jnp.where(mine >= shift, got_last, -1)
        got = (got_state, got_last)
        excl = combine_states(got, excl)
        if 2 * shift < count:
            incl = combine_states(got, incl)
        shift *= 2
    return excl


def on_device(queries, keys, values, segment_ids):
    rows = queries.shape[0]
    heads = queries.shape[1] // DH
    blocks = rows // BLK
    q_all = queries.reshape(blocks, BLK, heads, DH)
    k_all = keys.reshape(blocks, BLK, heads, DH)
    v_all = values.reshape(blocks, BLK, heads, DH)
    s_all = segment_ids.reshape(blocks, BLK)
    positions = jnp.arange(BLK)
    causal = positions[:, None] >= positions[None, :]

    def local_block(item):
        qb, kb, vb, sb = item
        scores = jnp.einsum("thd,shd->hts", qb, kb, preferred_element_type=jnp.float32)
        mask = causal & (sb[:, None] == sb[None, :])
        probs = jnp.where(mask[None], scores, 0.0).astype(jnp.bfloat16)
        intra = jnp.einsum("hts,shd->thd", probs, vb, preferred_element_type=jnp.float32)
        block_last = sb[-1]
        keep = (sb == block_last)[:, None, None]
        kv_sum = jnp.einsum(
            "thd,the->hde",
            jnp.where(keep, kb, jnp.zeros_like(kb)),
            vb,
            preferred_element_type=jnp.float32,
        )
        return (intra, kv_sum, block_last)

    intra_all, kv_all, last_all = lax.map(local_block, (q_all, k_all, v_all, s_all))
    empty_state = (jnp.zeros((heads, DH, DH), jnp.float32), jnp.int32(-1))

    def fold_local(carry, item):
        return (combine_states(carry, item), None)

    own_state, _ = lax.scan(fold_local, empty_state, (kv_all, last_all))
    prefix = carried_in(own_state, "ctx")

    def inter_block(carry, item):
        qb, sb, kv_sum, block_last = item
        state, last = carry
        inter = jnp.einsum(
            "thd,hde->the", qb, state.astype(jnp.bfloat16), preferred_element_type=jnp.float32
        )
        inter = jnp.where((sb == last)[:, None, None], inter, 0.0)
        return (combine_states(carry, (kv_sum, block_last)), inter)

    _, inter_all = lax.scan(inter_block, prefix, (q_all, s_all, kv_all, last_all))
    outputs = (intra_all + inter_all).reshape(rows, heads * DH)
    squares = jnp.sum(outputs * outputs, axis=1)
    totals = lax.psum(squares, "head")
    scaled = outputs * lax.rsqrt(totals / (HEADS * DH) + 1e-05)[:, None]
    return scaled.astype(jnp.bfloat16)


def solution(mesh):
    in_specs = (P("ctx", "head"), P("ctx", "head"), P("ctx", "head"), P("ctx"))
    out_specs = P("ctx", "head")
    return jax.shard_map(
        on_device, mesh=mesh, in_specs=in_specs, out_specs=out_specs, check_vma=False
    )
```

```python
import jax
import jax.numpy as jnp
from jax import lax
from jax.sharding import Mesh
from jax.sharding import PartitionSpec as P

HEADS = 64
DH = 128
BLK = 512
TAG = 8


def combine_states(earlier, later):
    state_e, last_e = earlier
    state_l, last_l = later
    joined = state_l + jnp.where(last_e == last_l, state_e, jnp.zeros_like(state_e))
    state = jnp.where(last_l < 0, state_e, joined)
    last = jnp.where(last_l < 0, last_e, last_l)
    return (state, last)


def pack(value):
    state, last = value
    tag = jnp.full((TAG, DH), last.astype(jnp.float32))
    return jnp.concatenate([state.reshape(-1, DH), tag], axis=0)


def unpack(packed):
    state = packed[:-TAG].reshape(-1, DH, DH)
    return (state, packed[-TAG, 0].astype(jnp.int32))


def swap_cores(value, core_axis):
    return unpack(lax.ppermute(pack(value), core_axis, [(0, 1), (1, 0)]))


def scan_chips(own, axis):
    count, mine = (lax.axis_size(axis), lax.axis_index(axis))
    state, last = own
    excl = (jnp.zeros_like(state), jnp.full_like(last, -1))
    incl = (state, last)
    shift = 1
    while shift < count:
        pairs = [(j, j + shift) for j in range(count - shift)]
        got_state, got_last = unpack(lax.ppermute(pack(incl), axis, pairs))
        got = (got_state, jnp.where(mine >= shift, got_last, -1))
        excl = combine_states(got, excl)
        if 2 * shift < count:
            incl = combine_states(got, incl)
        shift *= 2
    return excl


def carried_in(own, chip_axis, core_axis):
    core = lax.axis_index(core_axis)
    other = swap_cores(own, core_axis)
    first = jax.tree.map(lambda a, b: jnp.where(core == 0, a, b), own, other)
    second = jax.tree.map(lambda a, b: jnp.where(core == 0, b, a), own, other)
    chip = combine_states(first, second)
    empty = (jnp.zeros_like(own[0]), jnp.full_like(own[1], -1))
    in_chip = jax.tree.map(lambda a, b: jnp.where(core == 0, a, b), empty, first)
    half = chip[0].shape[0] // 2
    mine = jnp.where(core == 0, chip[0][:half], chip[0][half:])
    before = scan_chips((mine, chip[1]), chip_axis)
    theirs = swap_cores(before, core_axis)
    whole = jnp.where(
        core == 0,
        jnp.concatenate([before[0], theirs[0]], axis=0),
        jnp.concatenate([theirs[0], before[0]], axis=0),
    )
    return combine_states((whole, before[1]), in_chip)


def head_sum(x, axis):
    count = lax.axis_size(axis)
    spread = jnp.broadcast_to(x[None], (count,) + x.shape)
    return jnp.sum(lax.all_to_all(spread, axis, 0, 0, tiled=True), axis=0)


def on_device(queries, keys, values, segment_ids):
    rows = queries.shape[0]
    heads = queries.shape[1] // DH
    blocks = rows // BLK
    q_all = queries.reshape(blocks, BLK, heads, DH)
    k_all = keys.reshape(blocks, BLK, heads, DH)
    v_all = values.reshape(blocks, BLK, heads, DH)
    s_all = segment_ids.reshape(blocks, BLK)
    positions = jnp.arange(BLK)
    causal = positions[:, None] >= positions[None, :]

    def local_block(item):
        qb, kb, vb, sb = item
        scores = jnp.einsum("thd,shd->hts", qb, kb, preferred_element_type=jnp.float32)
        mask = causal & (sb[:, None] == sb[None, :])
        probs = jnp.where(mask[None], scores, 0.0).astype(jnp.bfloat16)
        intra = jnp.einsum("hts,shd->thd", probs, vb, preferred_element_type=jnp.float32)
        block_last = sb[-1]
        keep = (sb == block_last)[:, None, None]
        kv_sum = jnp.einsum(
            "thd,the->hde",
            jnp.where(keep, kb, jnp.zeros_like(kb)),
            vb,
            preferred_element_type=jnp.float32,
        )
        return (intra, kv_sum, block_last)

    intra_all, kv_all, last_all = lax.map(local_block, (q_all, k_all, v_all, s_all))
    empty_state = (jnp.zeros((heads, DH, DH), jnp.float32), jnp.int32(-1))

    def fold_local(carry, item):
        return (combine_states(carry, item), None)

    own_state, _ = lax.scan(fold_local, empty_state, (kv_all, last_all))
    prefix = carried_in(own_state, "chip", "core")

    def inter_block(carry, item):
        qb, sb, kv_sum, block_last = item
        state, last = carry
        inter = jnp.einsum(
            "thd,hde->the", qb, state.astype(jnp.bfloat16), preferred_element_type=jnp.float32
        )
        inter = jnp.where((sb == last)[:, None, None], inter, 0.0)
        return (combine_states(carry, (kv_sum, block_last)), inter)

    _, inter_all = lax.scan(inter_block, prefix, (q_all, s_all, kv_all, last_all))
    outputs = (intra_all + inter_all).reshape(rows, heads * DH)
    squares = jnp.sum(outputs * outputs, axis=1)
    totals = head_sum(squares, "head")
    scaled = outputs * lax.rsqrt(totals / (HEADS * DH) + 1e-05)[:, None]
    return scaled.astype(jnp.bfloat16)


def solution(mesh):
    ctx, head = (mesh.shape["ctx"], mesh.shape["head"])
    split = Mesh(mesh.devices.reshape(ctx // 2, 2, head), ("chip", "core", "head"))
    rows = P(("chip", "core"), "head")
    in_specs = (rows, rows, rows, P(("chip", "core")))
    return jax.shard_map(on_device, mesh=split, in_specs=in_specs, out_specs=rows, check_vma=False)
```

```python
import jax
import jax.numpy as jnp
from jax import lax
from jax.sharding import Mesh
from jax.sharding import PartitionSpec as P

HEADS = 64
DH = 128
BLK = 512
TAG = 8
GROUP = 4


def combine_states(earlier, later):
    state_e, last_e = earlier
    state_l, last_l = later
    joined = state_l + jnp.where(last_e == last_l, state_e, jnp.zeros_like(state_e))
    state = jnp.where(last_l < 0, state_e, joined)
    last = jnp.where(last_l < 0, last_e, last_l)
    return (state, last)


def pack(value):
    state, last = value
    tag = jnp.full((TAG, DH), last.astype(jnp.float32))
    return jnp.concatenate([state.reshape(-1, DH), tag], axis=0)


def unpack(packed):
    state = packed[:-TAG].reshape(-1, DH, DH)
    return (state, packed[-TAG, 0].astype(jnp.int32))


def swap_cores(value, core_axis):
    return unpack(lax.ppermute(pack(value), core_axis, [(0, 1), (1, 0)]))


def received(value, axis, pairs, valid):
    state, last = unpack(lax.ppermute(pack(value), axis, pairs))
    return (jnp.where(valid, state, 0.0), jnp.where(valid, last, -1))


def select(cond, a, b):
    return jax.tree.map(lambda x, y: jnp.where(cond, x, y), a, b)


def scan_chips(own, axis):
    count, mine = (lax.axis_size(axis), lax.axis_index(axis))
    group = GROUP if count % GROUP == 0 else 1
    groups = count // group
    offset, which = (mine % group, mine // group)
    empty = (jnp.zeros_like(own[0]), jnp.full_like(own[1], -1))
    incl, excl = (own, empty)
    shift = 1
    while shift < group:
        pairs = [(j, j + shift) for j in range(count - shift) if j % group + shift < group]
        got = received(incl, axis, pairs, offset >= shift)
        excl = combine_states(got, excl)
        incl = combine_states(got, incl)
        shift *= 2
    ends = [group * j + group - 1 for j in range(groups)]
    upto, before = (incl, empty)
    shift = 1
    while shift < groups:
        pairs = [(ends[j], ends[j + shift]) for j in range(groups - shift)]
        got = received(upto, axis, pairs, which >= shift)
        before = combine_states(got, before)
        if 2 * shift < groups:
            upto = combine_states(got, upto)
        shift *= 2
    through = combine_states(before, incl)
    carried = before
    for place in range(group - 1):
        ahead = place + 1
        behind = group - 1 - place
        if ahead <= behind:
            pairs = [(ends[j], ends[j] + ahead) for j in range(groups - 1)]
            got = received(through, axis, pairs, which >= 1)
        else:
            pairs = [(ends[j], ends[j] - behind) for j in range(groups)]
            got = received(before, axis, pairs, which >= 0)
        carried = select(offset == place, got, carried)
    return combine_states(carried, excl)


def carried_in(own, chip_axis, core_axis):
    core = lax.axis_index(core_axis)
    other = swap_cores(own, core_axis)
    first = jax.tree.map(lambda a, b: jnp.where(core == 0, a, b), own, other)
    second = jax.tree.map(lambda a, b: jnp.where(core == 0, b, a), own, other)
    chip = combine_states(first, second)
    empty = (jnp.zeros_like(own[0]), jnp.full_like(own[1], -1))
    in_chip = jax.tree.map(lambda a, b: jnp.where(core == 0, a, b), empty, first)
    half = chip[0].shape[0] // 2
    mine = jnp.where(core == 0, chip[0][:half], chip[0][half:])
    before = scan_chips((mine, chip[1]), chip_axis)
    theirs = swap_cores(before, core_axis)
    whole = jnp.where(
        core == 0,
        jnp.concatenate([before[0], theirs[0]], axis=0),
        jnp.concatenate([theirs[0], before[0]], axis=0),
    )
    return combine_states((whole, before[1]), in_chip)


def head_sum(x, axis):
    count = lax.axis_size(axis)
    spread = jnp.broadcast_to(x[None], (count,) + x.shape)
    return jnp.sum(lax.all_to_all(spread, axis, 0, 0, tiled=True), axis=0)


def on_device(queries, keys, values, segment_ids):
    rows = queries.shape[0]
    heads = queries.shape[1] // DH
    blocks = rows // BLK
    q_all = queries.reshape(blocks, BLK, heads, DH)
    k_all = keys.reshape(blocks, BLK, heads, DH)
    v_all = values.reshape(blocks, BLK, heads, DH)
    s_all = segment_ids.reshape(blocks, BLK)
    positions = jnp.arange(BLK)
    causal = positions[:, None] >= positions[None, :]

    def local_block(item):
        qb, kb, vb, sb = item
        scores = jnp.einsum("thd,shd->hts", qb, kb, preferred_element_type=jnp.float32)
        mask = causal & (sb[:, None] == sb[None, :])
        probs = jnp.where(mask[None], scores, 0.0).astype(jnp.bfloat16)
        intra = jnp.einsum("hts,shd->thd", probs, vb, preferred_element_type=jnp.float32)
        block_last = sb[-1]
        keep = (sb == block_last)[:, None, None]
        kv_sum = jnp.einsum(
            "thd,the->hde",
            jnp.where(keep, kb, jnp.zeros_like(kb)),
            vb,
            preferred_element_type=jnp.float32,
        )
        return (intra, kv_sum, block_last)

    intra_all, kv_all, last_all = lax.map(local_block, (q_all, k_all, v_all, s_all))
    empty_state = (jnp.zeros((heads, DH, DH), jnp.float32), jnp.int32(-1))

    def fold_local(carry, item):
        return (combine_states(carry, item), None)

    own_state, _ = lax.scan(fold_local, empty_state, (kv_all, last_all))
    prefix = carried_in(own_state, "chip", "core")

    def inter_block(carry, item):
        qb, sb, kv_sum, block_last = item
        state, last = carry
        inter = jnp.einsum(
            "thd,hde->the", qb, state.astype(jnp.bfloat16), preferred_element_type=jnp.float32
        )
        inter = jnp.where((sb == last)[:, None, None], inter, 0.0)
        return (combine_states(carry, (kv_sum, block_last)), inter)

    _, inter_all = lax.scan(inter_block, prefix, (q_all, s_all, kv_all, last_all))
    outputs = (intra_all + inter_all).reshape(rows, heads * DH)
    squares = jnp.sum(outputs * outputs, axis=1)
    totals = head_sum(squares, "head")
    scaled = outputs * lax.rsqrt(totals / (HEADS * DH) + 1e-05)[:, None]
    return scaled.astype(jnp.bfloat16)


def solution(mesh):
    ctx, head = (mesh.shape["ctx"], mesh.shape["head"])
    split = Mesh(mesh.devices.reshape(ctx // 2, 2, head), ("chip", "core", "head"))
    rows = P(("chip", "core"), "head")
    in_specs = (rows, rows, rows, P(("chip", "core")))
    return jax.shard_map(on_device, mesh=split, in_specs=in_specs, out_specs=rows, check_vma=False)
```

```python
import jax
import jax.numpy as jnp
from jax import lax
from jax.sharding import Mesh
from jax.sharding import PartitionSpec as P

HEADS = 64
DH = 128
BLK = 512
TAG = 8
GROUP = 4


def combine_states(earlier, later):
    state_e, last_e = earlier
    state_l, last_l = later
    joined = state_l + jnp.where(last_e == last_l, state_e, jnp.zeros_like(state_e))
    state = jnp.where(last_l < 0, state_e, joined)
    last = jnp.where(last_l < 0, last_e, last_l)
    return (state, last)


def pack(value):
    state, last = value
    tag = jnp.full((TAG, DH), last.astype(jnp.float32))
    return jnp.concatenate([state.reshape(-1, DH), tag], axis=0)


def unpack(packed):
    state = packed[:-TAG].reshape(-1, DH, DH)
    return (state, packed[-TAG, 0].astype(jnp.int32))


def tag_of(packed):
    return packed[-TAG:-TAG + 1, :1]


def combine_packed(earlier, later):
    last_e, last_l = (tag_of(earlier), tag_of(later))
    is_tag = lax.broadcasted_iota(jnp.int32, later.shape, 0) >= later.shape[0] - TAG
    joined = later + jnp.where(last_e == last_l, earlier, 0.0)
    return jnp.where(last_l < 0, earlier, jnp.where(is_tag, later, joined))


def empty_like(packed):
    is_tag = lax.broadcasted_iota(jnp.int32, packed.shape, 0) >= packed.shape[0] - TAG
    return jnp.where(is_tag, -1.0, 0.0).astype(packed.dtype)


def received(packed, axis, pairs, valid):
    return jnp.where(valid, lax.ppermute(packed, axis, pairs), empty_like(packed))


def scan_chips(own, axis):
    count, mine = (lax.axis_size(axis), lax.axis_index(axis))
    group = GROUP if count % GROUP == 0 else 1
    groups = count // group
    offset, which = (mine % group, mine // group)
    empty = empty_like(own)
    incl, excl = (own, empty)
    shift = 1
    while shift < group:
        pairs = [(j, j + shift) for j in range(count - shift) if j % group + shift < group]
        got = received(incl, axis, pairs, offset >= shift)
        excl = combine_packed(got, excl)
        incl = combine_packed(got, incl)
        shift *= 2
    ends = [group * j + group - 1 for j in range(groups)]
    upto, before = (incl, empty)
    shift = 1
    while shift < groups:
        pairs = [(ends[j], ends[j + shift]) for j in range(groups - shift)]
        got = received(upto, axis, pairs, which >= shift)
        before = combine_packed(got, before)
        if 2 * shift < groups:
            upto = combine_packed(got, upto)
        shift *= 2
    through = combine_packed(before, incl)
    carried = before
    for place in range(group - 1):
        ahead = place + 1
        behind = group - 1 - place
        if ahead <= behind:
            pairs = [(ends[j], ends[j] + ahead) for j in range(groups - 1)]
            got = received(through, axis, pairs, which >= 1)
        else:
            pairs = [(ends[j], ends[j] - behind) for j in range(groups)]
            got = received(before, axis, pairs, which >= 0)
        carried = jnp.where(offset == place, got, carried)
    return combine_packed(carried, excl)


def carried_in(own, chip_axis, core_axis):
    core = lax.axis_index(core_axis)
    swap = [(0, 1), (1, 0)]
    own_p = pack(own)
    other = lax.ppermute(own_p, core_axis, swap)
    first = jnp.where(core == 0, own_p, other)
    second = jnp.where(core == 0, other, own_p)
    chip = combine_packed(first, second)
    in_chip = jnp.where(core == 0, empty_like(own_p), first)
    rows = own[0].shape[0] * DH // 2
    tag = chip[-TAG:]
    mine = jnp.where(
        core == 0,
        jnp.concatenate([chip[:rows], tag], axis=0),
        jnp.concatenate([chip[rows:2 * rows], tag], axis=0),
    )
    before = scan_chips(mine, chip_axis)
    theirs = lax.ppermute(before, core_axis, swap)
    whole = jnp.where(
        core == 0,
        jnp.concatenate([before[:rows], theirs[:rows], before[rows:]], axis=0),
        jnp.concatenate([theirs[:rows], before[:rows], before[rows:]], axis=0),
    )
    return unpack(combine_packed(whole, in_chip))


def head_sum(x, axis):
    count = lax.axis_size(axis)
    spread = jnp.broadcast_to(x[None], (count,) + x.shape)
    return jnp.sum(lax.all_to_all(spread, axis, 0, 0, tiled=True), axis=0)


def on_device(queries, keys, values, segment_ids):
    rows = queries.shape[0]
    heads = queries.shape[1] // DH
    blocks = rows // BLK
    q_all = queries.reshape(blocks, BLK, heads, DH)
    k_all = keys.reshape(blocks, BLK, heads, DH)
    v_all = values.reshape(blocks, BLK, heads, DH)
    s_all = segment_ids.reshape(blocks, BLK)
    positions = jnp.arange(BLK)
    causal = positions[:, None] >= positions[None, :]

    def local_block(item):
        qb, kb, vb, sb = item
        scores = jnp.einsum("thd,shd->hts", qb, kb, preferred_element_type=jnp.float32)
        mask = causal & (sb[:, None] == sb[None, :])
        probs = jnp.where(mask[None], scores, 0.0).astype(jnp.bfloat16)
        intra = jnp.einsum("hts,shd->thd", probs, vb, preferred_element_type=jnp.float32)
        block_last = sb[-1]
        keep = (sb == block_last)[:, None, None]
        kv_sum = jnp.einsum(
            "thd,the->hde",
            jnp.where(keep, kb, jnp.zeros_like(kb)),
            vb,
            preferred_element_type=jnp.float32,
        )
        return (intra, kv_sum, block_last)

    def inter_of(qb, sb, state, last):
        inter = jnp.einsum(
            "thd,hde->the", qb, state.astype(jnp.bfloat16), preferred_element_type=jnp.float32
        )
        return jnp.where((sb == last)[:, None, None], inter, 0.0)

    if blocks == 1:
        intra, kv_sum, block_last = local_block((q_all[0], k_all[0], v_all[0], s_all[0]))
        state, last = carried_in((kv_sum, block_last), "chip", "core")
        outputs = (intra + inter_of(q_all[0], s_all[0], state, last)).reshape(rows, heads * DH)
    else:
        intra_all, kv_all, last_all = lax.map(local_block, (q_all, k_all, v_all, s_all))
        empty_state = (jnp.zeros((heads, DH, DH), jnp.float32), jnp.int32(-1))

        def fold_local(carry, item):
            return (combine_states(carry, item), None)

        own_state, _ = lax.scan(fold_local, empty_state, (kv_all, last_all))
        prefix = carried_in(own_state, "chip", "core")

        def inter_block(carry, item):
            qb, sb, kv_sum, block_last = item
            inter = inter_of(qb, sb, *carry)
            return (combine_states(carry, (kv_sum, block_last)), inter)

        _, inter_all = lax.scan(inter_block, prefix, (q_all, s_all, kv_all, last_all))
        outputs = (intra_all + inter_all).reshape(rows, heads * DH)
    squares = jnp.sum(outputs * outputs, axis=1)
    totals = head_sum(squares, "head")
    scaled = outputs * lax.rsqrt(totals / (HEADS * DH) + 1e-05)[:, None]
    return scaled.astype(jnp.bfloat16)


def solution(mesh):
    ctx, head = (mesh.shape["ctx"], mesh.shape["head"])
    split = Mesh(mesh.devices.reshape(ctx // 2, 2, head), ("chip", "core", "head"))
    rows = P(("chip", "core"), "head")
    in_specs = (rows, rows, rows, P(("chip", "core")))
    return jax.shard_map(on_device, mesh=split, in_specs=in_specs, out_specs=rows, check_vma=False)
```

```python
import jax
import jax.numpy as jnp
from jax import lax
from jax.sharding import Mesh
from jax.sharding import PartitionSpec as P

HEADS = 64
DH = 128
BLK = 512
TAG = 8
GROUP = 4


def combine_states(earlier, later):
    state_e, last_e = earlier
    state_l, last_l = later
    joined = state_l + jnp.where(last_e == last_l, state_e, jnp.zeros_like(state_e))
    state = jnp.where(last_l < 0, state_e, joined)
    last = jnp.where(last_l < 0, last_e, last_l)
    return (state, last)


def pack(value):
    state, last = value
    tag = jnp.full((TAG, DH), last.astype(jnp.float32))
    return jnp.concatenate([state.reshape(-1, DH), tag], axis=0)


def unpack(packed):
    state = packed[:-TAG].reshape(-1, DH, DH)
    return (state, packed[-TAG, 0].astype(jnp.int32))


def swap_cores(value, core_axis):
    return unpack(lax.ppermute(pack(value), core_axis, [(0, 1), (1, 0)]))


def received(value, axis, pairs, valid):
    state, last = unpack(lax.ppermute(pack(value), axis, pairs))
    return (jnp.where(valid, state, 0.0), jnp.where(valid, last, -1))


def select(cond, a, b):
    return jax.tree.map(lambda x, y: jnp.where(cond, x, y), a, b)


def scan_chips(own, axis):
    count, mine = (lax.axis_size(axis), lax.axis_index(axis))
    group = GROUP if count % GROUP == 0 else 1
    groups = count // group
    offset, which = (mine % group, mine // group)
    empty = (jnp.zeros_like(own[0]), jnp.full_like(own[1], -1))
    incl, excl = (own, empty)
    shift = 1
    while shift < group:
        pairs = [(j, j + shift) for j in range(count - shift) if j % group + shift < group]
        got = received(incl, axis, pairs, offset >= shift)
        excl = combine_states(got, excl)
        incl = combine_states(got, incl)
        shift *= 2
    ends = [group * j + group - 1 for j in range(groups)]
    upto, before = (incl, empty)
    shift = 1
    while shift < groups:
        pairs = [(ends[j], ends[j + shift]) for j in range(groups - shift)]
        got = received(upto, axis, pairs, which >= shift)
        before = combine_states(got, before)
        if 2 * shift < groups:
            upto = combine_states(got, upto)
        shift *= 2
    through = combine_states(before, incl)
    carried = before
    for place in range(group - 1):
        ahead = place + 1
        behind = group - 1 - place
        if ahead <= behind:
            pairs = [(ends[j], ends[j] + ahead) for j in range(groups - 1)]
            got = received(through, axis, pairs, which >= 1)
        else:
            pairs = [(ends[j], ends[j] - behind) for j in range(groups)]
            got = received(before, axis, pairs, which >= 0)
        carried = select(offset == place, got, carried)
    return combine_states(carried, excl)


def carried_in(own, chip_axis, core_axis):
    core = lax.axis_index(core_axis)
    other = swap_cores(own, core_axis)
    first = jax.tree.map(lambda a, b: jnp.where(core == 0, a, b), own, other)
    second = jax.tree.map(lambda a, b: jnp.where(core == 0, b, a), own, other)
    chip = combine_states(first, second)
    empty = (jnp.zeros_like(own[0]), jnp.full_like(own[1], -1))
    in_chip = jax.tree.map(lambda a, b: jnp.where(core == 0, a, b), empty, first)
    half = chip[0].shape[0] // 2
    mine = jnp.where(core == 0, chip[0][:half], chip[0][half:])
    parts = [scan_chips((mine[i:i + 1], chip[1]), chip_axis) for i in range(half)]
    before = (jnp.concatenate([p[0] for p in parts], axis=0), parts[0][1])
    theirs = swap_cores(before, core_axis)
    whole = jnp.where(
        core == 0,
        jnp.concatenate([before[0], theirs[0]], axis=0),
        jnp.concatenate([theirs[0], before[0]], axis=0),
    )
    return combine_states((whole, before[1]), in_chip)


def head_sum(x, axis):
    count = lax.axis_size(axis)
    spread = jnp.broadcast_to(x[None], (count,) + x.shape)
    return jnp.sum(lax.all_to_all(spread, axis, 0, 0, tiled=True), axis=0)


def on_device(queries, keys, values, segment_ids):
    rows = queries.shape[0]
    heads = queries.shape[1] // DH
    blocks = rows // BLK
    q_all = queries.reshape(blocks, BLK, heads, DH)
    k_all = keys.reshape(blocks, BLK, heads, DH)
    v_all = values.reshape(blocks, BLK, heads, DH)
    s_all = segment_ids.reshape(blocks, BLK)
    positions = jnp.arange(BLK)
    causal = positions[:, None] >= positions[None, :]

    def local_block(item):
        qb, kb, vb, sb = item
        scores = jnp.einsum("thd,shd->hts", qb, kb, preferred_element_type=jnp.float32)
        mask = causal & (sb[:, None] == sb[None, :])
        probs = jnp.where(mask[None], scores, 0.0).astype(jnp.bfloat16)
        intra = jnp.einsum("hts,shd->thd", probs, vb, preferred_element_type=jnp.float32)
        block_last = sb[-1]
        keep = (sb == block_last)[:, None, None]
        kv_sum = jnp.einsum(
            "thd,the->hde",
            jnp.where(keep, kb, jnp.zeros_like(kb)),
            vb,
            preferred_element_type=jnp.float32,
        )
        return (intra, kv_sum, block_last)

    intra_all, kv_all, last_all = lax.map(local_block, (q_all, k_all, v_all, s_all))
    empty_state = (jnp.zeros((heads, DH, DH), jnp.float32), jnp.int32(-1))

    def fold_local(carry, item):
        return (combine_states(carry, item), None)

    own_state, _ = lax.scan(fold_local, empty_state, (kv_all, last_all))
    prefix = carried_in(own_state, "chip", "core")

    def inter_block(carry, item):
        qb, sb, kv_sum, block_last = item
        state, last = carry
        inter = jnp.einsum(
            "thd,hde->the", qb, state.astype(jnp.bfloat16), preferred_element_type=jnp.float32
        )
        inter = jnp.where((sb == last)[:, None, None], inter, 0.0)
        return (combine_states(carry, (kv_sum, block_last)), inter)

    _, inter_all = lax.scan(inter_block, prefix, (q_all, s_all, kv_all, last_all))
    outputs = (intra_all + inter_all).reshape(rows, heads * DH)
    squares = jnp.sum(outputs * outputs, axis=1)
    totals = head_sum(squares, "head")
    scaled = outputs * lax.rsqrt(totals / (HEADS * DH) + 1e-05)[:, None]
    return scaled.astype(jnp.bfloat16)


def solution(mesh):
    ctx, head = (mesh.shape["ctx"], mesh.shape["head"])
    split = Mesh(mesh.devices.reshape(ctx // 2, 2, head), ("chip", "core", "head"))
    rows = P(("chip", "core"), "head")
    in_specs = (rows, rows, rows, P(("chip", "core")))
    return jax.shard_map(on_device, mesh=split, in_specs=in_specs, out_specs=rows, check_vma=False)
```

```python
import jax
import jax.numpy as jnp
from jax import lax
from jax.sharding import Mesh
from jax.sharding import PartitionSpec as P

HEADS = 64
DH = 128
BLK = 512
TAG = 8
GROUP = 4


def combine_states(earlier, later):
    state_e, last_e = earlier
    state_l, last_l = later
    joined = state_l + jnp.where(last_e == last_l, state_e, jnp.zeros_like(state_e))
    state = jnp.where(last_l < 0, state_e, joined)
    last = jnp.where(last_l < 0, last_e, last_l)
    return (state, last)


def pack(value):
    state, last = value
    tag = jnp.full((TAG, DH), last.astype(jnp.float32))
    return jnp.concatenate([state.reshape(-1, DH), tag], axis=0)


def unpack(packed):
    state = packed[:-TAG].reshape(-1, DH, DH)
    return (state, packed[-TAG, 0].astype(jnp.int32))


def swap_cores(value, core_axis):
    return unpack(lax.ppermute(pack(value), core_axis, [(0, 1), (1, 0)]))


def received(value, axis, pairs, valid):
    state, last = unpack(lax.ppermute(pack(value), axis, pairs))
    return (jnp.where(valid, state, 0.0), jnp.where(valid, last, -1))


def select(cond, a, b):
    return jax.tree.map(lambda x, y: jnp.where(cond, x, y), a, b)


def scan_chips(own, axis):
    count, mine = (lax.axis_size(axis), lax.axis_index(axis))
    group = GROUP if count % GROUP == 0 else 1
    groups = count // group
    offset, which = (mine % group, mine // group)
    empty = (jnp.zeros_like(own[0]), jnp.full_like(own[1], -1))
    incl, excl = (own, empty)
    shift = 1
    while shift < group:
        pairs = [(j, j + shift) for j in range(count - shift) if j % group + shift < group]
        got = received(incl, axis, pairs, offset >= shift)
        excl = combine_states(got, excl)
        incl = combine_states(got, incl)
        shift *= 2
    ends = [group * j + group - 1 for j in range(groups)]
    upto, before = (incl, empty)
    shift = 1
    while shift < groups:
        pairs = [(ends[j], ends[j + shift]) for j in range(groups - shift)]
        got = received(upto, axis, pairs, which >= shift)
        before = combine_states(got, before)
        if 2 * shift < groups:
            upto = combine_states(got, upto)
        shift *= 2
    through = pack(combine_states(before, incl))
    carried = pack(before)
    for place in range(group - 1):
        ahead = place + 1
        behind = group - 1 - place
        if ahead <= behind:
            pairs = [(ends[j], ends[j] + ahead) for j in range(groups - 1)]
            got = lax.ppermute(through, axis, pairs)
            got = jnp.where(which >= 1, got, pack(empty))
        else:
            pairs = [(ends[j], ends[j] - behind) for j in range(groups)]
            got = lax.ppermute(carried, axis, pairs)
        carried = jnp.where(offset == place, got, carried)
    return combine_states(unpack(carried), excl)


def carried_in(own, chip_axis, core_axis):
    core = lax.axis_index(core_axis)
    other = swap_cores(own, core_axis)
    first = jax.tree.map(lambda a, b: jnp.where(core == 0, a, b), own, other)
    second = jax.tree.map(lambda a, b: jnp.where(core == 0, b, a), own, other)
    chip = combine_states(first, second)
    empty = (jnp.zeros_like(own[0]), jnp.full_like(own[1], -1))
    in_chip = jax.tree.map(lambda a, b: jnp.where(core == 0, a, b), empty, first)
    half = chip[0].shape[0] // 2
    mine = jnp.where(core == 0, chip[0][:half], chip[0][half:])
    before = scan_chips((mine, chip[1]), chip_axis)
    theirs = swap_cores(before, core_axis)
    whole = jnp.where(
        core == 0,
        jnp.concatenate([before[0], theirs[0]], axis=0),
        jnp.concatenate([theirs[0], before[0]], axis=0),
    )
    return combine_states((whole, before[1]), in_chip)


def head_sum(x, axis):
    count = lax.axis_size(axis)
    spread = jnp.broadcast_to(x[None], (count,) + x.shape)
    return jnp.sum(lax.all_to_all(spread, axis, 0, 0, tiled=True), axis=0)


def on_device(queries, keys, values, segment_ids):
    rows = queries.shape[0]
    heads = queries.shape[1] // DH
    blocks = rows // BLK
    q_all = queries.reshape(blocks, BLK, heads, DH)
    k_all = keys.reshape(blocks, BLK, heads, DH)
    v_all = values.reshape(blocks, BLK, heads, DH)
    s_all = segment_ids.reshape(blocks, BLK)
    positions = jnp.arange(BLK)
    causal = positions[:, None] >= positions[None, :]

    def local_block(item):
        qb, kb, vb, sb = item
        scores = jnp.einsum("thd,shd->hts", qb, kb, preferred_element_type=jnp.float32)
        mask = causal & (sb[:, None] == sb[None, :])
        probs = jnp.where(mask[None], scores, 0.0).astype(jnp.bfloat16)
        intra = jnp.einsum("hts,shd->thd", probs, vb, preferred_element_type=jnp.float32)
        block_last = sb[-1]
        keep = (sb == block_last)[:, None, None]
        kv_sum = jnp.einsum(
            "thd,the->hde",
            jnp.where(keep, kb, jnp.zeros_like(kb)),
            vb,
            preferred_element_type=jnp.float32,
        )
        return (intra, kv_sum, block_last)

    intra_all, kv_all, last_all = lax.map(local_block, (q_all, k_all, v_all, s_all))
    empty_state = (jnp.zeros((heads, DH, DH), jnp.float32), jnp.int32(-1))

    def fold_local(carry, item):
        return (combine_states(carry, item), None)

    own_state, _ = lax.scan(fold_local, empty_state, (kv_all, last_all))
    prefix = carried_in(own_state, "chip", "core")

    def inter_block(carry, item):
        qb, sb, kv_sum, block_last = item
        state, last = carry
        inter = jnp.einsum(
            "thd,hde->the", qb, state.astype(jnp.bfloat16), preferred_element_type=jnp.float32
        )
        inter = jnp.where((sb == last)[:, None, None], inter, 0.0)
        return (combine_states(carry, (kv_sum, block_last)), inter)

    _, inter_all = lax.scan(inter_block, prefix, (q_all, s_all, kv_all, last_all))
    outputs = (intra_all + inter_all).reshape(rows, heads * DH)
    squares = jnp.sum(outputs * outputs, axis=1)
    totals = head_sum(squares, "head")
    scaled = outputs * lax.rsqrt(totals / (HEADS * DH) + 1e-05)[:, None]
    return scaled.astype(jnp.bfloat16)


def solution(mesh):
    ctx, head = (mesh.shape["ctx"], mesh.shape["head"])
    split = Mesh(mesh.devices.reshape(ctx // 2, 2, head), ("chip", "core", "head"))
    rows = P(("chip", "core"), "head")
    in_specs = (rows, rows, rows, P(("chip", "core")))
    return jax.shard_map(on_device, mesh=split, in_specs=in_specs, out_specs=rows, check_vma=False)
```

```python
import jax
import jax.numpy as jnp
from jax import lax
from jax.sharding import Mesh
from jax.sharding import PartitionSpec as P

HEADS = 64
DH = 128
BLK = 512
TAG = 8
GROUP = 4


def combine_states(earlier, later):
    state_e, last_e = earlier
    state_l, last_l = later
    joined = state_l + jnp.where(last_e == last_l, state_e, jnp.zeros_like(state_e))
    state = jnp.where(last_l < 0, state_e, joined)
    last = jnp.where(last_l < 0, last_e, last_l)
    return (state, last)


def pack(value):
    state, last = value
    tag = jnp.full((TAG, DH), last.astype(jnp.float32))
    return jnp.concatenate([state.reshape(-1, DH), tag], axis=0)


def unpack(packed):
    state = packed[:-TAG].reshape(-1, DH, DH)
    return (state, packed[-TAG, 0].astype(jnp.int32))


def swap_cores(value, core_axis):
    return unpack(lax.ppermute(pack(value), core_axis, [(0, 1), (1, 0)]))


def received(value, axis, pairs, valid):
    state, last = unpack(lax.ppermute(pack(value), axis, pairs))
    return (jnp.where(valid, state, 0.0), jnp.where(valid, last, -1))


def select(cond, a, b):
    return jax.tree.map(lambda x, y: jnp.where(cond, x, y), a, b)


def scan_chips(own, axis):
    count, mine = (lax.axis_size(axis), lax.axis_index(axis))
    group = GROUP if count % GROUP == 0 else 1
    groups = count // group
    offset, which = (mine % group, mine // group)
    empty = (jnp.zeros_like(own[0]), jnp.full_like(own[1], -1))
    excl = empty
    for shift in range(group - 1, 0, -1):
        pairs = [(j, j + shift) for j in range(count - shift) if j % group + shift < group]
        excl = combine_states(excl, received(own, axis, pairs, offset >= shift))
    incl = combine_states(excl, own)
    ends = [group * j + group - 1 for j in range(groups)]
    upto, before = (incl, empty)
    shift = 1
    while shift < groups:
        pairs = [(ends[j], ends[j + shift]) for j in range(groups - shift)]
        got = received(upto, axis, pairs, which >= shift)
        before = combine_states(got, before)
        if 2 * shift < groups:
            upto = combine_states(got, upto)
        shift *= 2
    through = pack(combine_states(before, incl))
    carried = pack(before)
    for place in range(group - 1):
        ahead = place + 1
        behind = group - 1 - place
        if ahead <= behind:
            pairs = [(ends[j], ends[j] + ahead) for j in range(groups - 1)]
            got = lax.ppermute(through, axis, pairs)
            got = jnp.where(which >= 1, got, pack(empty))
        else:
            pairs = [(ends[j], ends[j] - behind) for j in range(groups)]
            got = lax.ppermute(carried, axis, pairs)
        carried = jnp.where(offset == place, got, carried)
    return combine_states(unpack(carried), excl)


def carried_in(own, chip_axis, core_axis):
    core = lax.axis_index(core_axis)
    other = swap_cores(own, core_axis)
    first = jax.tree.map(lambda a, b: jnp.where(core == 0, a, b), own, other)
    second = jax.tree.map(lambda a, b: jnp.where(core == 0, b, a), own, other)
    chip = combine_states(first, second)
    empty = (jnp.zeros_like(own[0]), jnp.full_like(own[1], -1))
    in_chip = jax.tree.map(lambda a, b: jnp.where(core == 0, a, b), empty, first)
    half = chip[0].shape[0] // 2
    mine = jnp.where(core == 0, chip[0][:half], chip[0][half:])
    before = scan_chips((mine, chip[1]), chip_axis)
    theirs = swap_cores(before, core_axis)
    whole = jnp.where(
        core == 0,
        jnp.concatenate([before[0], theirs[0]], axis=0),
        jnp.concatenate([theirs[0], before[0]], axis=0),
    )
    return combine_states((whole, before[1]), in_chip)


def head_sum(x, axis):
    count = lax.axis_size(axis)
    spread = jnp.broadcast_to(x[None], (count,) + x.shape)
    return jnp.sum(lax.all_to_all(spread, axis, 0, 0, tiled=True), axis=0)


def on_device(queries, keys, values, segment_ids):
    rows = queries.shape[0]
    heads = queries.shape[1] // DH
    blocks = rows // BLK
    q_all = queries.reshape(blocks, BLK, heads, DH)
    k_all = keys.reshape(blocks, BLK, heads, DH)
    v_all = values.reshape(blocks, BLK, heads, DH)
    s_all = segment_ids.reshape(blocks, BLK)
    positions = jnp.arange(BLK)
    causal = positions[:, None] >= positions[None, :]

    def local_block(item):
        qb, kb, vb, sb = item
        scores = jnp.einsum("thd,shd->hts", qb, kb, preferred_element_type=jnp.float32)
        mask = causal & (sb[:, None] == sb[None, :])
        probs = jnp.where(mask[None], scores, 0.0).astype(jnp.bfloat16)
        intra = jnp.einsum("hts,shd->thd", probs, vb, preferred_element_type=jnp.float32)
        block_last = sb[-1]
        keep = (sb == block_last)[:, None, None]
        kv_sum = jnp.einsum(
            "thd,the->hde",
            jnp.where(keep, kb, jnp.zeros_like(kb)),
            vb,
            preferred_element_type=jnp.float32,
        )
        return (intra, kv_sum, block_last)

    intra_all, kv_all, last_all = lax.map(local_block, (q_all, k_all, v_all, s_all))
    empty_state = (jnp.zeros((heads, DH, DH), jnp.float32), jnp.int32(-1))

    def fold_local(carry, item):
        return (combine_states(carry, item), None)

    own_state, _ = lax.scan(fold_local, empty_state, (kv_all, last_all))
    prefix = carried_in(own_state, "chip", "core")

    def inter_block(carry, item):
        qb, sb, kv_sum, block_last = item
        state, last = carry
        inter = jnp.einsum(
            "thd,hde->the", qb, state.astype(jnp.bfloat16), preferred_element_type=jnp.float32
        )
        inter = jnp.where((sb == last)[:, None, None], inter, 0.0)
        return (combine_states(carry, (kv_sum, block_last)), inter)

    _, inter_all = lax.scan(inter_block, prefix, (q_all, s_all, kv_all, last_all))
    outputs = (intra_all + inter_all).reshape(rows, heads * DH)
    squares = jnp.sum(outputs * outputs, axis=1)
    totals = head_sum(squares, "head")
    scaled = outputs * lax.rsqrt(totals / (HEADS * DH) + 1e-05)[:, None]
    return scaled.astype(jnp.bfloat16)


def solution(mesh):
    ctx, head = (mesh.shape["ctx"], mesh.shape["head"])
    split = Mesh(mesh.devices.reshape(ctx // 2, 2, head), ("chip", "core", "head"))
    rows = P(("chip", "core"), "head")
    in_specs = (rows, rows, rows, P(("chip", "core")))
    return jax.shard_map(on_device, mesh=split, in_specs=in_specs, out_specs=rows, check_vma=False)
```

```python
import jax
import jax.numpy as jnp
from jax import lax
from jax.sharding import Mesh
from jax.sharding import PartitionSpec as P

HEADS = 64
DH = 128
BLK = 512
TAG = 8
GROUP = 4


def combine_states(earlier, later):
    state_e, last_e = earlier
    state_l, last_l = later
    joined = state_l + jnp.where(last_e == last_l, state_e, jnp.zeros_like(state_e))
    state = jnp.where(last_l < 0, state_e, joined)
    last = jnp.where(last_l < 0, last_e, last_l)
    return (state, last)


def pack(value):
    state, last = value
    tag = jnp.full((TAG, DH), last.astype(jnp.float32))
    return jnp.concatenate([state.reshape(-1, DH), tag], axis=0)


def unpack(packed):
    state = packed[:-TAG].reshape(-1, DH, DH)
    return (state, packed[-TAG, 0].astype(jnp.int32))


def swap_cores(value, core_axis):
    return unpack(lax.ppermute(pack(value), core_axis, [(0, 1), (1, 0)]))


def received(value, axis, pairs, valid):
    state, last = unpack(lax.ppermute(pack(value), axis, pairs))
    return (jnp.where(valid, state, 0.0), jnp.where(valid, last, -1))


def select(cond, a, b):
    return jax.tree.map(lambda x, y: jnp.where(cond, x, y), a, b)


def group_prefix(total, axis, ends, which, empty):
    count, groups = (lax.axis_size(axis), len(ends))
    half = groups // 2
    upto, before, back = (total, empty, total)
    shift = 1
    while shift < half:
        pairs = [(ends[j - shift], ends[j]) for j in range(groups) if j % half >= shift]
        got = received(upto, axis, pairs, which % half >= shift)
        before = combine_states(got, before)
        upto = combine_states(got, upto)
        pairs = [(ends[j + shift], ends[j]) for j in range(half - shift)]
        back = combine_states(back, received(back, axis, pairs, which + shift < half))
        shift *= 2
    source = pack(select(which == 0, back, upto))
    ahead = [g for g in range(half, groups) if ends[g] - ends[half - 1] <= count - ends[g] + ends[0]]
    behind = [g for g in range(half, groups) if g not in ahead]
    lower = pack(empty)
    for k in range(max(len(ahead), len(behind))):
        pairs, hit = ([], jnp.zeros((), jnp.bool_))
        if k < len(ahead):
            pairs.append((ends[half - 1], ends[ahead[k]]))
            hit = hit | (which == ahead[k])
        if k < len(behind):
            pairs.append((ends[0], ends[behind[k]]))
            hit = hit | (which == behind[k])
        lower = jnp.where(hit, lax.ppermute(source, axis, pairs), lower)
    lower = unpack(lower)
    return (combine_states(lower, before), combine_states(lower, upto))


def scan_chips(own, axis):
    count, mine = (lax.axis_size(axis), lax.axis_index(axis))
    group = GROUP if count % GROUP == 0 else 1
    groups = count // group
    offset, which = (mine % group, mine // group)
    empty = (jnp.zeros_like(own[0]), jnp.full_like(own[1], -1))
    excl = empty
    for shift in range(group - 1, 0, -1):
        pairs = [(j, j + shift) for j in range(count - shift) if j % group + shift < group]
        excl = combine_states(excl, received(own, axis, pairs, offset >= shift))
    incl = combine_states(excl, own)
    ends = [group * j + group - 1 for j in range(groups)]
    if groups >= 4 and groups % 2 == 0:
        before, through = group_prefix(incl, axis, ends, which, empty)
    else:
        upto, before = (incl, empty)
        shift = 1
        while shift < groups:
            pairs = [(ends[j], ends[j + shift]) for j in range(groups - shift)]
            got = received(upto, axis, pairs, which >= shift)
            before = combine_states(got, before)
            if 2 * shift < groups:
                upto = combine_states(got, upto)
            shift *= 2
        through = combine_states(before, incl)
    through = pack(through)
    carried = pack(before)
    for place in range(group - 1):
        ahead = place + 1
        behind = group - 1 - place
        if ahead <= behind:
            pairs = [(ends[j], ends[j] + ahead) for j in range(groups - 1)]
            got = lax.ppermute(through, axis, pairs)
            got = jnp.where(which >= 1, got, pack(empty))
        else:
            pairs = [(ends[j], ends[j] - behind) for j in range(groups)]
            got = lax.ppermute(carried, axis, pairs)
        carried = jnp.where(offset == place, got, carried)
    return combine_states(unpack(carried), excl)


def carried_in(own, chip_axis, core_axis):
    core = lax.axis_index(core_axis)
    other = swap_cores(own, core_axis)
    first = jax.tree.map(lambda a, b: jnp.where(core == 0, a, b), own, other)
    second = jax.tree.map(lambda a, b: jnp.where(core == 0, b, a), own, other)
    chip = combine_states(first, second)
    empty = (jnp.zeros_like(own[0]), jnp.full_like(own[1], -1))
    in_chip = jax.tree.map(lambda a, b: jnp.where(core == 0, a, b), empty, first)
    half = chip[0].shape[0] // 2
    mine = jnp.where(core == 0, chip[0][:half], chip[0][half:])
    before = scan_chips((mine, chip[1]), chip_axis)
    theirs = swap_cores(before, core_axis)
    whole = jnp.where(
        core == 0,
        jnp.concatenate([before[0], theirs[0]], axis=0),
        jnp.concatenate([theirs[0], before[0]], axis=0),
    )
    return combine_states((whole, before[1]), in_chip)


def head_sum(x, axis):
    count = lax.axis_size(axis)
    spread = jnp.broadcast_to(x[None], (count,) + x.shape)
    return jnp.sum(lax.all_to_all(spread, axis, 0, 0, tiled=True), axis=0)


def on_device(queries, keys, values, segment_ids):
    rows = queries.shape[0]
    heads = queries.shape[1] // DH
    blocks = rows // BLK
    q_all = queries.reshape(blocks, BLK, heads, DH)
    k_all = keys.reshape(blocks, BLK, heads, DH)
    v_all = values.reshape(blocks, BLK, heads, DH)
    s_all = segment_ids.reshape(blocks, BLK)
    positions = jnp.arange(BLK)
    causal = positions[:, None] >= positions[None, :]

    def local_block(item):
        qb, kb, vb, sb = item
        scores = jnp.einsum("thd,shd->hts", qb, kb, preferred_element_type=jnp.float32)
        mask = causal & (sb[:, None] == sb[None, :])
        probs = jnp.where(mask[None], scores, 0.0).astype(jnp.bfloat16)
        intra = jnp.einsum("hts,shd->thd", probs, vb, preferred_element_type=jnp.float32)
        block_last = sb[-1]
        keep = (sb == block_last)[:, None, None]
        kv_sum = jnp.einsum(
            "thd,the->hde",
            jnp.where(keep, kb, jnp.zeros_like(kb)),
            vb,
            preferred_element_type=jnp.float32,
        )
        return (intra, kv_sum, block_last)

    intra_all, kv_all, last_all = lax.map(local_block, (q_all, k_all, v_all, s_all))
    empty_state = (jnp.zeros((heads, DH, DH), jnp.float32), jnp.int32(-1))

    def fold_local(carry, item):
        return (combine_states(carry, item), None)

    own_state, _ = lax.scan(fold_local, empty_state, (kv_all, last_all))
    prefix = carried_in(own_state, "chip", "core")

    def inter_block(carry, item):
        qb, sb, kv_sum, block_last = item
        state, last = carry
        inter = jnp.einsum(
            "thd,hde->the", qb, state.astype(jnp.bfloat16), preferred_element_type=jnp.float32
        )
        inter = jnp.where((sb == last)[:, None, None], inter, 0.0)
        return (combine_states(carry, (kv_sum, block_last)), inter)

    _, inter_all = lax.scan(inter_block, prefix, (q_all, s_all, kv_all, last_all))
    outputs = (intra_all + inter_all).reshape(rows, heads * DH)
    squares = jnp.sum(outputs * outputs, axis=1)
    totals = head_sum(squares, "head")
    scaled = outputs * lax.rsqrt(totals / (HEADS * DH) + 1e-05)[:, None]
    return scaled.astype(jnp.bfloat16)


def solution(mesh):
    ctx, head = (mesh.shape["ctx"], mesh.shape["head"])
    split = Mesh(mesh.devices.reshape(ctx // 2, 2, head), ("chip", "core", "head"))
    rows = P(("chip", "core"), "head")
    in_specs = (rows, rows, rows, P(("chip", "core")))
    return jax.shard_map(on_device, mesh=split, in_specs=in_specs, out_specs=rows, check_vma=False)
```

```python
import jax
import jax.numpy as jnp
from jax import lax
from jax.sharding import Mesh
from jax.sharding import PartitionSpec as P

HEADS = 64
DH = 128
BLK = 512
TAG = 8
GROUP = 4


def combine_states(earlier, later):
    state_e, last_e = earlier
    state_l, last_l = later
    joined = state_l + jnp.where(last_e == last_l, state_e, jnp.zeros_like(state_e))
    state = jnp.where(last_l < 0, state_e, joined)
    last = jnp.where(last_l < 0, last_e, last_l)
    return (state, last)


def pack(value):
    state, last = value
    tag = jnp.full((TAG, DH), last.astype(jnp.float32))
    return jnp.concatenate([state.reshape(-1, DH), tag], axis=0)


def unpack(packed):
    state = packed[:-TAG].reshape(-1, DH, DH)
    return (state, packed[-TAG, 0].astype(jnp.int32))


def swap_cores(value, core_axis):
    return unpack(lax.ppermute(pack(value), core_axis, [(0, 1), (1, 0)]))


def received(value, axis, pairs, valid):
    state, last = unpack(lax.ppermute(pack(value), axis, pairs))
    return (jnp.where(valid, state, 0.0), jnp.where(valid, last, -1))


def select(cond, a, b):
    return jax.tree.map(lambda x, y: jnp.where(cond, x, y), a, b)


def group_prefix(total, axis, ends, which, empty):
    count, groups = (lax.axis_size(axis), len(ends))
    half = groups // 2
    upto, before, back = (total, empty, total)
    shift = 1
    while shift < half:
        pairs = [(ends[j - shift], ends[j]) for j in range(groups) if j % half >= shift]
        got = received(upto, axis, pairs, which % half >= shift)
        before = combine_states(got, before)
        upto = combine_states(got, upto)
        pairs = [(ends[j + shift], ends[j]) for j in range(half - shift)]
        back = combine_states(back, received(back, axis, pairs, which + shift < half))
        shift *= 2
    source = pack(select(which == 0, back, upto))
    ahead = [g for g in range(half, groups) if ends[g] - ends[half - 1] <= count - ends[g] + ends[0]]
    behind = [g for g in range(half, groups) if g not in ahead]
    lower = pack(empty)
    for k in range(max(len(ahead), len(behind))):
        pairs, hit = ([], jnp.zeros((), jnp.bool_))
        if k < len(ahead):
            pairs.append((ends[half - 1], ends[ahead[k]]))
            hit = hit | (which == ahead[k])
        if k < len(behind):
            pairs.append((ends[0], ends[behind[k]]))
            hit = hit | (which == behind[k])
        lower = jnp.where(hit, lax.ppermute(source, axis, pairs), lower)
    lower = unpack(lower)
    return (combine_states(lower, before), combine_states(lower, upto))


def scan_chips(own, axis, core_axis):
    count, mine = (lax.axis_size(axis), lax.axis_index(axis))
    group = GROUP if count % GROUP == 0 else 1
    groups = count // group
    offset, which = (mine % group, mine // group)
    empty = (jnp.zeros_like(own[0]), jnp.full_like(own[1], -1))
    excl = empty
    for shift in range(group - 1, 0, -1):
        pairs = [(j, j + shift) for j in range(count - shift) if j % group + shift < group]
        excl = combine_states(excl, received(own, axis, pairs, offset >= shift))
    incl = combine_states(excl, own)
    ends = [group * j + group - 1 for j in range(groups)]
    if groups >= 4 and groups % 2 == 0:
        before, through = group_prefix(incl, axis, ends, which, empty)
    else:
        upto, before = (incl, empty)
        shift = 1
        while shift < groups:
            pairs = [(ends[j], ends[j + shift]) for j in range(groups - shift)]
            got = received(upto, axis, pairs, which >= shift)
            before = combine_states(got, before)
            if 2 * shift < groups:
                upto = combine_states(got, upto)
            shift *= 2
        through = combine_states(before, incl)
    through = pack(through)
    both = (axis, core_axis)
    core = lax.axis_index(core_axis)
    excl_other = swap_cores(excl, core_axis)
    mine_p = pack(before)
    carried, carried_other = (mine_p, lax.ppermute(mine_p, core_axis, [(0, 1), (1, 0)]))
    for place in range(group - 1):
        ahead = place + 1
        behind = group - 1 - place
        if ahead <= behind:
            pairs = [(ends[j], ends[j] + ahead) for j in range(groups - 1)]
            sent, valid = (through, which >= 1)
        else:
            pairs = [(ends[j], ends[j] - behind) for j in range(groups)]
            sent, valid = (mine_p, which >= 0)
        straight = [(2 * s + c, 2 * t + c) for s, t in pairs for c in range(2)]
        crossed = [(2 * s + c, 2 * t + 1 - c) for s, t in pairs for c in range(2)]
        got = jnp.where(valid, lax.ppermute(sent, both, straight), pack(empty))
        got_other = jnp.where(valid, lax.ppermute(sent, both, crossed), pack(empty))
        carried = jnp.where(offset == place, got, carried)
        carried_other = jnp.where(offset == place, got_other, carried_other)
    done = combine_states(unpack(carried), excl)
    done_other = combine_states(unpack(carried_other), excl_other)
    whole = jnp.where(
        core == 0,
        jnp.concatenate([done[0], done_other[0]], axis=0),
        jnp.concatenate([done_other[0], done[0]], axis=0),
    )
    return (whole, done[1])


def carried_in(own, chip_axis, core_axis):
    core = lax.axis_index(core_axis)
    other = swap_cores(own, core_axis)
    first = jax.tree.map(lambda a, b: jnp.where(core == 0, a, b), own, other)
    second = jax.tree.map(lambda a, b: jnp.where(core == 0, b, a), own, other)
    chip = combine_states(first, second)
    empty = (jnp.zeros_like(own[0]), jnp.full_like(own[1], -1))
    in_chip = jax.tree.map(lambda a, b: jnp.where(core == 0, a, b), empty, first)
    half = chip[0].shape[0] // 2
    mine = jnp.where(core == 0, chip[0][:half], chip[0][half:])
    return combine_states(scan_chips((mine, chip[1]), chip_axis, core_axis), in_chip)


def head_sum(x, axis):
    count = lax.axis_size(axis)
    spread = jnp.broadcast_to(x[None], (count,) + x.shape)
    return jnp.sum(lax.all_to_all(spread, axis, 0, 0, tiled=True), axis=0)


def on_device(queries, keys, values, segment_ids):
    rows = queries.shape[0]
    heads = queries.shape[1] // DH
    blocks = rows // BLK
    q_all = queries.reshape(blocks, BLK, heads, DH)
    k_all = keys.reshape(blocks, BLK, heads, DH)
    v_all = values.reshape(blocks, BLK, heads, DH)
    s_all = segment_ids.reshape(blocks, BLK)
    positions = jnp.arange(BLK)
    causal = positions[:, None] >= positions[None, :]

    def local_block(item):
        qb, kb, vb, sb = item
        scores = jnp.einsum("thd,shd->hts", qb, kb, preferred_element_type=jnp.float32)
        mask = causal & (sb[:, None] == sb[None, :])
        probs = jnp.where(mask[None], scores, 0.0).astype(jnp.bfloat16)
        intra = jnp.einsum("hts,shd->thd", probs, vb, preferred_element_type=jnp.float32)
        block_last = sb[-1]
        keep = (sb == block_last)[:, None, None]
        kv_sum = jnp.einsum(
            "thd,the->hde",
            jnp.where(keep, kb, jnp.zeros_like(kb)),
            vb,
            preferred_element_type=jnp.float32,
        )
        return (intra, kv_sum, block_last)

    intra_all, kv_all, last_all = lax.map(local_block, (q_all, k_all, v_all, s_all))
    empty_state = (jnp.zeros((heads, DH, DH), jnp.float32), jnp.int32(-1))

    def fold_local(carry, item):
        return (combine_states(carry, item), None)

    own_state, _ = lax.scan(fold_local, empty_state, (kv_all, last_all))
    prefix = carried_in(own_state, "chip", "core")

    def inter_block(carry, item):
        qb, sb, kv_sum, block_last = item
        state, last = carry
        inter = jnp.einsum(
            "thd,hde->the", qb, state.astype(jnp.bfloat16), preferred_element_type=jnp.float32
        )
        inter = jnp.where((sb == last)[:, None, None], inter, 0.0)
        return (combine_states(carry, (kv_sum, block_last)), inter)

    _, inter_all = lax.scan(inter_block, prefix, (q_all, s_all, kv_all, last_all))
    outputs = (intra_all + inter_all).reshape(rows, heads * DH)
    squares = jnp.sum(outputs * outputs, axis=1)
    totals = head_sum(squares, "head")
    scaled = outputs * lax.rsqrt(totals / (HEADS * DH) + 1e-05)[:, None]
    return scaled.astype(jnp.bfloat16)


def solution(mesh):
    ctx, head = (mesh.shape["ctx"], mesh.shape["head"])
    split = Mesh(mesh.devices.reshape(ctx // 2, 2, head), ("chip", "core", "head"))
    rows = P(("chip", "core"), "head")
    in_specs = (rows, rows, rows, P(("chip", "core")))
    return jax.shard_map(on_device, mesh=split, in_specs=in_specs, out_specs=rows, check_vma=False)
```

```python
import jax
import jax.numpy as jnp
from jax import lax
from jax.sharding import Mesh
from jax.sharding import PartitionSpec as P

HEADS = 64
DH = 128
BLK = 512
TAG = 8
GROUP = 4


def combine_states(earlier, later):
    state_e, last_e = earlier
    state_l, last_l = later
    joined = state_l + jnp.where(last_e == last_l, state_e, jnp.zeros_like(state_e))
    state = jnp.where(last_l < 0, state_e, joined)
    last = jnp.where(last_l < 0, last_e, last_l)
    return (state, last)


def pack(value):
    state, last = value
    tag = jnp.full((TAG, DH), last.astype(jnp.float32))
    return jnp.concatenate([state.reshape(-1, DH), tag], axis=0)


def unpack(packed):
    state = packed[:-TAG].reshape(-1, DH, DH)
    return (state, packed[-TAG, 0].astype(jnp.int32))


def swap_cores(value, core_axis):
    return unpack(lax.ppermute(pack(value), core_axis, [(0, 1), (1, 0)]))


def received(value, axis, pairs, valid):
    state, last = unpack(lax.ppermute(pack(value), axis, pairs))
    return (jnp.where(valid, state, 0.0), jnp.where(valid, last, -1))


def select(cond, a, b):
    return jax.tree.map(lambda x, y: jnp.where(cond, x, y), a, b)


def group_prefix(total, axis, ends, which, empty):
    count, groups = (lax.axis_size(axis), len(ends))
    half = groups // 2
    upto, before, back = (total, empty, total)
    shift = 1
    while shift < half:
        pairs = [(ends[j - shift], ends[j]) for j in range(groups) if j % half >= shift]
        got = received(upto, axis, pairs, which % half >= shift)
        before = combine_states(got, before)
        upto = combine_states(got, upto)
        pairs = [(ends[j + shift], ends[j]) for j in range(half - shift)]
        back = combine_states(back, received(back, axis, pairs, which + shift < half))
        shift *= 2
    source = pack(select(which == 0, back, upto))
    ahead = [g for g in range(half, groups) if ends[g] - ends[half - 1] <= count - ends[g] + ends[0]]
    behind = [g for g in range(half, groups) if g not in ahead]
    ahead = sorted(ahead, key=lambda g: ends[g] - ends[half - 1])
    behind = sorted(behind, key=lambda g: ends[0] - ends[g] + count)
    lower = pack(empty)
    for k in range(max(len(ahead), len(behind))):
        pairs, hit = ([], jnp.zeros((), jnp.bool_))
        if k < len(ahead):
            pairs.append((ends[half - 1], ends[ahead[k]]))
            hit = hit | (which == ahead[k])
        if k < len(behind):
            pairs.append((ends[0], ends[behind[k]]))
            hit = hit | (which == behind[k])
        lower = jnp.where(hit, lax.ppermute(source, axis, pairs), lower)
    lower = unpack(lower)
    return (combine_states(lower, before), combine_states(lower, upto))


def scan_chips(own, axis):
    count, mine = (lax.axis_size(axis), lax.axis_index(axis))
    group = GROUP if count % GROUP == 0 else 1
    groups = count // group
    offset, which = (mine % group, mine // group)
    empty = (jnp.zeros_like(own[0]), jnp.full_like(own[1], -1))
    excl = empty
    for shift in range(group - 1, 0, -1):
        pairs = [(j, j + shift) for j in range(count - shift) if j % group + shift < group]
        excl = combine_states(excl, received(own, axis, pairs, offset >= shift))
    incl = combine_states(excl, own)
    ends = [group * j + group - 1 for j in range(groups)]
    if groups >= 4 and groups % 2 == 0:
        before, through = group_prefix(incl, axis, ends, which, empty)
    else:
        upto, before = (incl, empty)
        shift = 1
        while shift < groups:
            pairs = [(ends[j], ends[j + shift]) for j in range(groups - shift)]
            got = received(upto, axis, pairs, which >= shift)
            before = combine_states(got, before)
            if 2 * shift < groups:
                upto = combine_states(got, upto)
            shift *= 2
        through = combine_states(before, incl)
    through = pack(through)
    carried = pack(before)
    for place in range(group - 1):
        ahead = place + 1
        behind = group - 1 - place
        if ahead <= behind:
            pairs = [(ends[j], ends[j] + ahead) for j in range(groups - 1)]
            got = lax.ppermute(through, axis, pairs)
            got = jnp.where(which >= 1, got, pack(empty))
        else:
            pairs = [(ends[j], ends[j] - behind) for j in range(groups)]
            got = lax.ppermute(carried, axis, pairs)
        carried = jnp.where(offset == place, got, carried)
    return combine_states(unpack(carried), excl)


def carried_in(own, chip_axis, core_axis):
    core = lax.axis_index(core_axis)
    other = swap_cores(own, core_axis)
    first = jax.tree.map(lambda a, b: jnp.where(core == 0, a, b), own, other)
    second = jax.tree.map(lambda a, b: jnp.where(core == 0, b, a), own, other)
    chip = combine_states(first, second)
    empty = (jnp.zeros_like(own[0]), jnp.full_like(own[1], -1))
    in_chip = jax.tree.map(lambda a, b: jnp.where(core == 0, a, b), empty, first)
    half = chip[0].shape[0] // 2
    mine = jnp.where(core == 0, chip[0][:half], chip[0][half:])
    before = scan_chips((mine, chip[1]), chip_axis)
    theirs = swap_cores(before, core_axis)
    whole = jnp.where(
        core == 0,
        jnp.concatenate([before[0], theirs[0]], axis=0),
        jnp.concatenate([theirs[0], before[0]], axis=0),
    )
    return combine_states((whole, before[1]), in_chip)


def head_sum(x, axis):
    count = lax.axis_size(axis)
    spread = jnp.broadcast_to(x[None], (count,) + x.shape)
    return jnp.sum(lax.all_to_all(spread, axis, 0, 0, tiled=True), axis=0)


def on_device(queries, keys, values, segment_ids):
    rows = queries.shape[0]
    heads = queries.shape[1] // DH
    blocks = rows // BLK
    q_all = queries.reshape(blocks, BLK, heads, DH)
    k_all = keys.reshape(blocks, BLK, heads, DH)
    v_all = values.reshape(blocks, BLK, heads, DH)
    s_all = segment_ids.reshape(blocks, BLK)
    positions = jnp.arange(BLK)
    causal = positions[:, None] >= positions[None, :]

    def local_block(item):
        qb, kb, vb, sb = item
        scores = jnp.einsum("thd,shd->hts", qb, kb, preferred_element_type=jnp.float32)
        mask = causal & (sb[:, None] == sb[None, :])
        probs = jnp.where(mask[None], scores, 0.0).astype(jnp.bfloat16)
        intra = jnp.einsum("hts,shd->thd", probs, vb, preferred_element_type=jnp.float32)
        block_last = sb[-1]
        keep = (sb == block_last)[:, None, None]
        kv_sum = jnp.einsum(
            "thd,the->hde",
            jnp.where(keep, kb, jnp.zeros_like(kb)),
            vb,
            preferred_element_type=jnp.float32,
        )
        return (intra, kv_sum, block_last)

    intra_all, kv_all, last_all = lax.map(local_block, (q_all, k_all, v_all, s_all))
    empty_state = (jnp.zeros((heads, DH, DH), jnp.float32), jnp.int32(-1))

    def fold_local(carry, item):
        return (combine_states(carry, item), None)

    own_state, _ = lax.scan(fold_local, empty_state, (kv_all, last_all))
    prefix = carried_in(own_state, "chip", "core")

    def inter_block(carry, item):
        qb, sb, kv_sum, block_last = item
        state, last = carry
        inter = jnp.einsum(
            "thd,hde->the", qb, state.astype(jnp.bfloat16), preferred_element_type=jnp.float32
        )
        inter = jnp.where((sb == last)[:, None, None], inter, 0.0)
        return (combine_states(carry, (kv_sum, block_last)), inter)

    _, inter_all = lax.scan(inter_block, prefix, (q_all, s_all, kv_all, last_all))
    outputs = (intra_all + inter_all).reshape(rows, heads * DH)
    squares = jnp.sum(outputs * outputs, axis=1)
    totals = head_sum(squares, "head")
    scaled = outputs * lax.rsqrt(totals / (HEADS * DH) + 1e-05)[:, None]
    return scaled.astype(jnp.bfloat16)


def solution(mesh):
    ctx, head = (mesh.shape["ctx"], mesh.shape["head"])
    split = Mesh(mesh.devices.reshape(ctx // 2, 2, head), ("chip", "core", "head"))
    rows = P(("chip", "core"), "head")
    in_specs = (rows, rows, rows, P(("chip", "core")))
    return jax.shard_map(on_device, mesh=split, in_specs=in_specs, out_specs=rows, check_vma=False)
```

```python
import jax
import jax.numpy as jnp
from jax import lax
from jax.sharding import Mesh
from jax.sharding import PartitionSpec as P

HEADS = 64
DH = 128
BLK = 512
TAG = 8
GROUP = 4


def combine_states(earlier, later):
    state_e, last_e = earlier
    state_l, last_l = later
    joined = state_l + jnp.where(last_e == last_l, state_e, jnp.zeros_like(state_e))
    state = jnp.where(last_l < 0, state_e, joined)
    last = jnp.where(last_l < 0, last_e, last_l)
    return (state, last)


def pack(value):
    state, last = value
    tag = jnp.full((TAG, DH), last.astype(jnp.float32))
    return jnp.concatenate([state.reshape(-1, DH), tag], axis=0)


def unpack(packed):
    state = packed[:-TAG].reshape(-1, DH, DH)
    return (state, packed[-TAG, 0].astype(jnp.int32))


def swap_cores(value, core_axis):
    return unpack(lax.ppermute(pack(value), core_axis, [(0, 1), (1, 0)]))


def received(value, axis, pairs, valid):
    state, last = unpack(lax.ppermute(pack(value), axis, pairs))
    return (jnp.where(valid, state, 0.0), jnp.where(valid, last, -1))


def select(cond, a, b):
    return jax.tree.map(lambda x, y: jnp.where(cond, x, y), a, b)


def group_prefix(total, axis, ends, which, empty):
    count, groups = (lax.axis_size(axis), len(ends))
    half = groups // 2
    upto, before, back = (total, empty, total)
    shift = 1
    while shift < half:
        pairs = [(ends[j - shift], ends[j]) for j in range(groups) if j % half >= shift]
        got = received(upto, axis, pairs, which % half >= shift)
        before = combine_states(got, before)
        upto = combine_states(got, upto)
        pairs = [(ends[j + shift], ends[j]) for j in range(half - shift)]
        back = combine_states(back, received(back, axis, pairs, which + shift < half))
        shift *= 2
    source = pack(select(which == 0, back, upto))
    ahead = [g for g in range(half, groups) if ends[g] - ends[half - 1] <= count - ends[g] + ends[0]]
    behind = [g for g in range(half, groups) if g not in ahead]
    lower = pack(empty)
    for k in range(max(len(ahead), len(behind))):
        pairs, hit = ([], jnp.zeros((), jnp.bool_))
        if k < len(ahead):
            pairs.append((ends[half - 1], ends[ahead[k]]))
            hit = hit | (which == ahead[k])
        if k < len(behind):
            pairs.append((ends[0], ends[behind[k]]))
            hit = hit | (which == behind[k])
        lower = jnp.where(hit, lax.ppermute(source, axis, pairs), lower)
    lower = unpack(lower)
    return (combine_states(lower, before), combine_states(lower, upto), before, upto, half)


def scan_chips(own, axis):
    count, mine = (lax.axis_size(axis), lax.axis_index(axis))
    group = GROUP if count % GROUP == 0 else 1
    groups = count // group
    offset, which = (mine % group, mine // group)
    empty = (jnp.zeros_like(own[0]), jnp.full_like(own[1], -1))
    excl = empty
    for shift in range(group - 1, 0, -1):
        pairs = [(j, j + shift) for j in range(count - shift) if j % group + shift < group]
        excl = combine_states(excl, received(own, axis, pairs, offset >= shift))
    incl = combine_states(excl, own)
    ends = [group * j + group - 1 for j in range(groups)]
    if groups >= 4 and groups % 2 == 0:
        before, through, early_before, early_through, split = group_prefix(incl, axis, ends, which, empty)
    else:
        upto, before = (incl, empty)
        shift = 1
        while shift < groups:
            pairs = [(ends[j], ends[j + shift]) for j in range(groups - shift)]
            got = received(upto, axis, pairs, which >= shift)
            before = combine_states(got, before)
            if 2 * shift < groups:
                upto = combine_states(got, upto)
            shift *= 2
        through = combine_states(before, incl)
        early_before, early_through, split = (before, through, groups)
    late = (pack(before), pack(through))
    early = (pack(early_before), pack(early_through))
    carried = late[0]
    for place in range(group - 1):
        ahead = place + 1
        behind = group - 1 - place
        if ahead <= behind:
            sources, step, kind = (range(groups - 1), ahead, 1)
        else:
            sources, step, kind = (range(groups), -behind, 0)
        got = pack(empty)
        for sent, chosen in ((early, [j for j in sources if j < split]), (late, [j for j in sources if j >= split])):
            if chosen:
                pairs = [(ends[j], ends[j] + step) for j in chosen]
                targets = [j + kind for j in chosen]
                hit = (which >= min(targets)) & (which <= max(targets))
                got = jnp.where(hit, lax.ppermute(sent[kind], axis, pairs), got)
        carried = jnp.where(offset == place, got, carried)
    return combine_states(unpack(carried), excl)


def carried_in(own, chip_axis, core_axis):
    core = lax.axis_index(core_axis)
    other = swap_cores(own, core_axis)
    first = jax.tree.map(lambda a, b: jnp.where(core == 0, a, b), own, other)
    second = jax.tree.map(lambda a, b: jnp.where(core == 0, b, a), own, other)
    chip = combine_states(first, second)
    empty = (jnp.zeros_like(own[0]), jnp.full_like(own[1], -1))
    in_chip = jax.tree.map(lambda a, b: jnp.where(core == 0, a, b), empty, first)
    half = chip[0].shape[0] // 2
    mine = jnp.where(core == 0, chip[0][:half], chip[0][half:])
    before = scan_chips((mine, chip[1]), chip_axis)
    theirs = swap_cores(before, core_axis)
    whole = jnp.where(
        core == 0,
        jnp.concatenate([before[0], theirs[0]], axis=0),
        jnp.concatenate([theirs[0], before[0]], axis=0),
    )
    return combine_states((whole, before[1]), in_chip)


def head_sum(x, axis):
    count = lax.axis_size(axis)
    spread = jnp.broadcast_to(x[None], (count,) + x.shape)
    return jnp.sum(lax.all_to_all(spread, axis, 0, 0, tiled=True), axis=0)


def on_device(queries, keys, values, segment_ids):
    rows = queries.shape[0]
    heads = queries.shape[1] // DH
    blocks = rows // BLK
    q_all = queries.reshape(blocks, BLK, heads, DH)
    k_all = keys.reshape(blocks, BLK, heads, DH)
    v_all = values.reshape(blocks, BLK, heads, DH)
    s_all = segment_ids.reshape(blocks, BLK)
    positions = jnp.arange(BLK)
    causal = positions[:, None] >= positions[None, :]

    def local_block(item):
        qb, kb, vb, sb = item
        scores = jnp.einsum("thd,shd->hts", qb, kb, preferred_element_type=jnp.float32)
        mask = causal & (sb[:, None] == sb[None, :])
        probs = jnp.where(mask[None], scores, 0.0).astype(jnp.bfloat16)
        intra = jnp.einsum("hts,shd->thd", probs, vb, preferred_element_type=jnp.float32)
        block_last = sb[-1]
        keep = (sb == block_last)[:, None, None]
        kv_sum = jnp.einsum(
            "thd,the->hde",
            jnp.where(keep, kb, jnp.zeros_like(kb)),
            vb,
            preferred_element_type=jnp.float32,
        )
        return (intra, kv_sum, block_last)

    intra_all, kv_all, last_all = lax.map(local_block, (q_all, k_all, v_all, s_all))
    empty_state = (jnp.zeros((heads, DH, DH), jnp.float32), jnp.int32(-1))

    def fold_local(carry, item):
        return (combine_states(carry, item), None)

    own_state, _ = lax.scan(fold_local, empty_state, (kv_all, last_all))
    prefix = carried_in(own_state, "chip", "core")

    def inter_block(carry, item):
        qb, sb, kv_sum, block_last = item
        state, last = carry
        inter = jnp.einsum(
            "thd,hde->the", qb, state.astype(jnp.bfloat16), preferred_element_type=jnp.float32
        )
        inter = jnp.where((sb == last)[:, None, None], inter, 0.0)
        return (combine_states(carry, (kv_sum, block_last)), inter)

    _, inter_all = lax.scan(inter_block, prefix, (q_all, s_all, kv_all, last_all))
    outputs = (intra_all + inter_all).reshape(rows, heads * DH)
    squares = jnp.sum(outputs * outputs, axis=1)
    totals = head_sum(squares, "head")
    scaled = outputs * lax.rsqrt(totals / (HEADS * DH) + 1e-05)[:, None]
    return scaled.astype(jnp.bfloat16)


def solution(mesh):
    ctx, head = (mesh.shape["ctx"], mesh.shape["head"])
    split = Mesh(mesh.devices.reshape(ctx // 2, 2, head), ("chip", "core", "head"))
    rows = P(("chip", "core"), "head")
    in_specs = (rows, rows, rows, P(("chip", "core")))
    return jax.shard_map(on_device, mesh=split, in_specs=in_specs, out_specs=rows, check_vma=False)
```
